128 devices in a mesh: grp: 8 (over x_hi, z), vocab: 16 (over y, x_lo, core).
Axes of the slice: x: 4 (x_hi: 2, x_lo: 2; x = x_hi * 2 + x_lo), y: 4, z: 4, core: 2. Of those that a mesh axis runs over, the one named last changes fastest.
Arguments:
- hidden: bfloat16 [1024, 8192], P('grp', 'vocab')
- head_weight: bfloat16 [81920, 8192], P(('grp', 'vocab'))
- targets: int32 [1024], replicated, may hold values from 0 to 81919
- old_logprobs: float32 [1024], replicated
- loss_mask: int32 [1024], replicated, may hold values 0 or 1
- beam_lengths: int32 [128], replicated, may hold values from 1 to 24, 1024 in all
- beam_group: int32 [128], replicated, may hold values from 0 to 1, as said below
- rewards: float32 [128], replicated, may hold values from 0 to 1, as said below
Outputs:
- logprob: float32 [1024], replicated
- total_loss: float32 [], replicated
- head_grad: bfloat16 [81920, 8192], P(('grp', 'vocab'))
The draws below stay inside these ranges and needn't reach their ends.
Inputs may be any that keep to these rules, and one draw needn't show every extreme that they name: `beam_group`: each of the 2 groups is named by exactly 64 beams. `rewards`: multiples of 1/8.
All inputs are finite; a program needn't handle non-finite values.
Results may differ from the reference program's by a relative error of at most 0.005.
Values may be sent and summed in bfloat16 or wider, within the bound.
No kernel may reach another device: no remote copies, remote signals or barrier semaphores. Data moves between devices by JAX's collectives and lax.ppermute only.
A program may use at most 128 MiB of HBM per device.

```python
import math
import jax
import jax.numpy as jnp
import numpy as np
from jax import lax

D = 8192
VOCAB = 81920
GROUP_BEAMS = 64
TOKENS = 1024
BEAMS = 128
MOST_LEN = 24


def draw_head_weight(key, part):
    scale = 3.0 / math.sqrt(D)
    base = jnp.clip(jax.random.normal(jax.random.fold_in(key, 1), (VOCAB, D), jnp.float32), -5.0, 5.0) * scale
    return base.astype(jnp.bfloat16)


def draw_hidden(key, part):
    base = jnp.clip(jax.random.normal(jax.random.fold_in(key, 2), (TOKENS, D), jnp.float32), -5.0, 5.0)
    return base.astype(jnp.bfloat16)


def draw_targets(key, part):
    picks = jax.random.randint(jax.random.fold_in(key, 41), (TOKENS,), 0, VOCAB).astype(jnp.int32)
    high_pos = jax.random.randint(jax.random.fold_in(key, 42), (), 0, TOKENS).astype(jnp.int32)
    low_pos = ((high_pos + TOKENS // 2) % TOKENS).astype(jnp.int32)
    picks = picks.at[high_pos].set(VOCAB - 1)
    picks = picks.at[low_pos].set(0)
    return picks.astype(jnp.int32)


def draw_old_logprobs(key, part):
    features = draw_hidden(key, part)
    weight = draw_head_weight(key, part)
    chosen = draw_targets(key, part)
    pieces = 16
    block_rows = VOCAB // pieces
    blocks = weight.reshape(pieces, block_rows, D)

    def block_logits(weight_block):
        return lax.dot_general(features, weight_block, (((1,), (1,)), ((), ())), preferred_element_type=jnp.float32)
    maxima = lax.map(lambda weight_block: jnp.max(block_logits(weight_block), axis=1), blocks)
    upper = jnp.max(maxima, axis=0)
    sums = lax.map(lambda weight_block: jnp.sum(jnp.exp(block_logits(weight_block) - upper[:, None]), axis=1), blocks)
    log_total = upper + jnp.log(jnp.sum(sums, axis=0))
    rows = weight[chosen].astype(jnp.float32)
    target_logit = jnp.sum(features.astype(jnp.float32) * rows, axis=1)
    offset = jax.random.uniform(jax.random.fold_in(key, 51), (TOKENS,), jnp.float32, -0.5, 0.5)
    return (target_logit - log_total - offset).astype(jnp.float32)


def draw_beam_group(key, part):
    return (jax.random.permutation(jax.random.fold_in(key, 31), BEAMS) // GROUP_BEAMS).astype(jnp.int32)


def draw_rewards(key, part):
    levels = jax.random.randint(jax.random.fold_in(key, 21), (BEAMS,), 0, 9)
    return levels.astype(jnp.float32) / 8.0


def plant(result, own_key, least, largest):
    shape = result.shape
    place = [jax.random.randint(jax.random.fold_in(own_key, axis), (), 0, shape[axis]) for axis in range(len(shape))]
    result = result.at[tuple(place)].set(least)
    longest = shape.index(max(shape))
    place[longest] = (place[longest] + 1) % shape[longest]
    return result.at[tuple(place)].set(largest)


def split_up(count, total, bound, slope):
    portions = [(1 << 20) // math.isqrt(rank ** slope) + 1 for rank in range(2, count + 1)]
    rest, given = total - bound - (count - 1), [1] * (count - 1)
    while rest > 0:
        free = [i for i in range(count - 1) if given[i] < bound]
        mass, budget = sum([portions[i] for i in free]), rest
        for i in free:
            addition = min(bound - given[i], max(1, budget * portions[i] // mass), rest)
            given[i] = given[i] + addition
            rest = rest - addition
    return np.array([bound] + given)


def ragged_sizes(stream_key, count, total, most, skew):
    if count == 2:
        one = jax.random.randint(stream_key, (), max(1, total - most), min(most, total - 1) + 1)
        return jnp.stack([one, total - one])
    sizes = jnp.asarray(split_up(count, total, most, skew), jnp.int32)
    twos = (count - 1) // 2
    donor, receiver = sizes[1:1 + 2 * twos:2], sizes[2:2 + 2 * twos:2]
    margin = jnp.minimum(donor - 1, most - receiver)
    moved = jax.random.randint(jax.random.fold_in(stream_key, 1), (twos,), 0, 1 << 20) % (margin + 1)
    sizes = sizes.at[1:1 + 2 * twos:2].set(donor - moved).at[2:2 + 2 * twos:2].set(receiver + moved)
    return sizes[jax.random.permutation(jax.random.fold_in(stream_key, 2), count)]


def setup_inputs(seed: int = 0) -> dict:
    seeds = jax.random.split(jax.random.key(seed), 9)
    hidden = draw_hidden(jax.random.fold_in(seeds[8], 71), 0)
    head_weight = draw_head_weight(jax.random.fold_in(seeds[8], 71), 0)
    targets = draw_targets(jax.random.fold_in(seeds[8], 71), 0)
    old_logprobs = draw_old_logprobs(jax.random.fold_in(seeds[8], 71), 0)
    loss_mask = plant((jax.random.randint(seeds[4], (TOKENS,), 0, 4) < 3).astype(jnp.int32), jax.random.fold_in(seeds[4], 1), 0, 1)
    beam_lengths = ragged_sizes(seeds[5], BEAMS, TOKENS, MOST_LEN, 2).astype(jnp.int32)
    beam_group = draw_beam_group(jax.random.fold_in(seeds[8], 71), 0)
    rewards = draw_rewards(jax.random.fold_in(seeds[8], 71), 0)
    return dict(hidden=hidden, head_weight=head_weight, targets=targets, old_logprobs=old_logprobs, loss_mask=loss_mask, beam_lengths=beam_lengths, beam_group=beam_group, rewards=rewards)


def policy_terms(logprob, old_logprobs, loss_mask, beam_lengths, beam_group, rewards):
    highest = lax.Precision.HIGHEST
    tok_count = logprob.shape[0]
    beam_count = beam_lengths.shape[0]
    group_count = beam_count // GROUP_BEAMS
    beam_ends = jnp.cumsum(beam_lengths).astype(jnp.int32)
    position = jnp.arange(tok_count, dtype=jnp.int32)
    beam_of = lax.optimization_barrier(jnp.sum((position[:, None] >= beam_ends[None, :]).astype(jnp.int32), axis=1))
    token_beam = (beam_of[:, None] == jnp.arange(beam_count, dtype=jnp.int32)[None, :]).astype(jnp.float32)
    beam_onehot = (beam_group[:, None] == jnp.arange(group_count, dtype=jnp.int32)[None, :]).astype(jnp.float32)
    group_mean = jnp.dot(rewards, beam_onehot, precision=highest) / GROUP_BEAMS
    centred = rewards - jnp.dot(beam_onehot, group_mean, precision=highest)
    group_var = jnp.dot(centred * centred, beam_onehot, precision=highest) / GROUP_BEAMS
    advantage = centred / jnp.sqrt(jnp.dot(beam_onehot, group_var, precision=highest) + 1e-06)
    weight = loss_mask.astype(jnp.float32)
    counts = jnp.dot(weight, token_beam, precision=highest)
    token_adv = jnp.dot(token_beam, advantage, precision=highest)
    token_norm = jnp.dot(token_beam, jnp.maximum(counts, 1.0), precision=highest)
    ratios = jnp.exp(logprob - old_logprobs)
    clipped = jnp.clip(ratios, 0.8, 1.2)
    plain_term = ratios * token_adv
    bounded = clipped * token_adv
    token_share = weight / token_norm
    total_loss = -jnp.sum(token_share * jnp.minimum(plain_term, bounded))
    slopes = -token_share * jnp.where(plain_term <= bounded, plain_term, 0.0)
    return (total_loss, slopes)

def reference(hidden, head_weight, targets, old_logprobs, loss_mask, beam_lengths, beam_group, rewards):
    pieces = 16
    block_rows = VOCAB // pieces
    weights = head_weight.reshape(pieces, block_rows, D)
    starts = (jnp.arange(pieces, dtype=jnp.int32) * block_rows).astype(jnp.int32)

    def block_logits(weight_block):
        return lax.dot_general(hidden, weight_block, (((1,), (1,)), ((), ())), preferred_element_type=jnp.float32)
    maxima = lax.map(lambda weight_block: lax.optimization_barrier(jnp.max(block_logits(weight_block), axis=1)), weights)
    top = lax.optimization_barrier(jnp.max(maxima, axis=0))

    def block_sums(items):
        weight_block, start = items
        logits = block_logits(weight_block)
        vocab_ids = start + jnp.arange(block_rows, dtype=jnp.int32)
        hits = targets[:, None] == vocab_ids[None, :]
        return (lax.optimization_barrier(jnp.sum(jnp.exp(logits - top[:, None]), axis=1)), lax.optimization_barrier(jnp.sum(jnp.where(hits, logits, 0.0), axis=1)))
    sums, picks = lax.map(block_sums, (weights, starts))
    log_total = top + jnp.log(lax.optimization_barrier(jnp.sum(sums, axis=0)))
    logprob = lax.optimization_barrier(jnp.sum(picks, axis=0)) - log_total
    total_loss, slopes = policy_terms(logprob, old_logprobs, loss_mask, beam_lengths, beam_group, rewards)

    def block_grad(items):
        weight_block, start = items
        logits = block_logits(weight_block)
        vocab_ids = start + jnp.arange(block_rows, dtype=jnp.int32)
        hits = (targets[:, None] == vocab_ids[None, :]).astype(jnp.float32)
        grads = (slopes[:, None] * (hits - jnp.exp(logits - log_total[:, None]))).astype(jnp.bfloat16)
        return lax.dot_general(grads, hidden, (((0,), (0,)), ((), ())), preferred_element_type=jnp.float32).astype(jnp.bfloat16)
    head_grad = lax.map(block_grad, (weights, starts)).reshape(VOCAB, D)
    return (logprob, total_loss, head_grad)
```

```python
import jax
import jax.numpy as jnp
from jax import lax
from jax.sharding import PartitionSpec as P

GROUP_BEAMS = 64


def policy_terms(logprob, old_logprobs, loss_mask, beam_lengths, beam_group, rewards):
    highest = lax.Precision.HIGHEST
    tok_count = logprob.shape[0]
    beam_count = beam_lengths.shape[0]
    group_count = beam_count // GROUP_BEAMS
    beam_ends = jnp.cumsum(beam_lengths)
    position = jnp.arange(tok_count, dtype=jnp.int32)
    beam_of = jnp.sum((position[:, None] >= beam_ends[None, :]).astype(jnp.int32), axis=1)
    token_beam = (beam_of[:, None] == jnp.arange(beam_count, dtype=jnp.int32)[None, :]).astype(
        jnp.float32
    )
    beam_onehot = (beam_group[:, None] == jnp.arange(group_count, dtype=jnp.int32)[None, :]).astype(
        jnp.float32
    )
    group_mean = jnp.dot(rewards, beam_onehot, precision=highest) / GROUP_BEAMS
    centred = rewards - jnp.dot(beam_onehot, group_mean, precision=highest)
    group_var = jnp.dot(centred * centred, beam_onehot, precision=highest) / GROUP_BEAMS
    advantage = centred / jnp.sqrt(jnp.dot(beam_onehot, group_var, precision=highest) + 1e-06)
    weight = loss_mask.astype(jnp.float32)
    counts = jnp.dot(weight, token_beam, precision=highest)
    token_adv = jnp.dot(token_beam, advantage, precision=highest)
    token_norm = jnp.dot(token_beam, jnp.maximum(counts, 1.0), precision=highest)
    ratios = jnp.exp(logprob - old_logprobs)
    clipped = jnp.clip(ratios, 0.8, 1.2)
    plain_term = ratios * token_adv
    bounded = clipped * token_adv
    token_share = weight / token_norm
    total_loss = -jnp.sum(token_share * jnp.minimum(plain_term, bounded))
    slopes = -token_share * jnp.where(plain_term <= bounded, plain_term, 0.0)
    return (total_loss, slopes)


def combine(mine, theirs):
    top = jnp.maximum(mine[0], theirs[0])
    total = mine[1] * jnp.exp(mine[0] - top) + theirs[1] * jnp.exp(theirs[0] - top)
    return jnp.stack([top, total, mine[2] + theirs[2]])


def butterfly(stats):
    for axis in ("vocab", "grp"):
        size = lax.axis_size(axis)
        step = 1
        while step < size:
            perm = [(i, i ^ step) for i in range(size)]
            stats = combine(stats, lax.ppermute(stats, axis, perm))
            step *= 2
    return stats[0], stats[1], stats[2]


def shards(
    hidden, head_weight, targets, old_logprobs, loss_mask, beam_lengths, beam_group, rewards
):
    token_block = lax.all_gather(hidden, "grp", axis=0, tiled=True)
    features = lax.all_gather(token_block, "vocab", axis=1, tiled=True)
    shard = head_weight.shape[0]
    offset = (lax.axis_index("grp") * lax.axis_size("vocab") + lax.axis_index("vocab")) * shard
    vocab_ids = offset + jnp.arange(shard, dtype=jnp.int32)
    logits = lax.dot_general(
        features, head_weight, (((1,), (1,)), ((), ())), preferred_element_type=jnp.float32
    )
    hits = targets[:, None] == vocab_ids[None, :]
    picked = jnp.sum(jnp.where(hits, logits, 0.0), axis=1)
    local_top = jnp.max(logits, axis=1)
    local_sum = jnp.sum(jnp.exp(logits - local_top[:, None]), axis=1)
    top, total, target_logit = butterfly(jnp.stack([local_top, local_sum, picked]))
    log_total = top + jnp.log(total)
    logprob = target_logit - log_total
    total_loss, slopes = policy_terms(
        logprob, old_logprobs, loss_mask, beam_lengths, beam_group, rewards
    )
    grads = (
        slopes[:, None] * (hits.astype(jnp.float32) - jnp.exp(logits - log_total[:, None]))
    ).astype(jnp.bfloat16)
    head_grad = lax.dot_general(
        grads, features, (((0,), (0,)), ((), ())), preferred_element_type=jnp.float32
    )
    return (logprob, total_loss, head_grad.astype(jnp.bfloat16))


def solution(mesh):
    in_specs = (P("grp", "vocab"), P(("grp", "vocab"), None), P(), P(), P(), P(), P(), P())
    out_specs = (P(), P(), P(("grp", "vocab"), None))
    return jax.shard_map(shards, mesh=mesh, in_specs=in_specs, out_specs=out_specs, check_vma=False)
```

```python
import jax
import jax.numpy as jnp
from jax import lax
from jax.sharding import PartitionSpec as P

GROUP_BEAMS = 64


def policy_terms(logprob, old_logprobs, loss_mask, beam_lengths, beam_group, rewards):
    highest = lax.Precision.HIGHEST
    tok_count = logprob.shape[0]
    beam_count = beam_lengths.shape[0]
    group_count = beam_count // GROUP_BEAMS
    beam_ends = jnp.cumsum(beam_lengths)
    position = jnp.arange(tok_count, dtype=jnp.int32)
    beam_of = jnp.sum((position[:, None] >= beam_ends[None, :]).astype(jnp.int32), axis=1)
    token_beam = (beam_of[:, None] == jnp.arange(beam_count, dtype=jnp.int32)[None, :]).astype(
        jnp.float32
    )
    beam_onehot = (beam_group[:, None] == jnp.arange(group_count, dtype=jnp.int32)[None, :]).astype(
        jnp.float32
    )
    group_mean = jnp.dot(rewards, beam_onehot, precision=highest) / GROUP_BEAMS
    centred = rewards - jnp.dot(beam_onehot, group_mean, precision=highest)
    group_var = jnp.dot(centred * centred, beam_onehot, precision=highest) / GROUP_BEAMS
    advantage = centred / jnp.sqrt(jnp.dot(beam_onehot, group_var, precision=highest) + 1e-06)
    weight = loss_mask.astype(jnp.float32)
    counts = jnp.dot(weight, token_beam, precision=highest)
    token_adv = jnp.dot(token_beam, advantage, precision=highest)
    token_norm = jnp.dot(token_beam, jnp.maximum(counts, 1.0), precision=highest)
    ratios = jnp.exp(logprob - old_logprobs)
    clipped = jnp.clip(ratios, 0.8, 1.2)
    plain_term = ratios * token_adv
    bounded = clipped * token_adv
    token_share = weight / token_norm
    total_loss = -jnp.sum(token_share * jnp.minimum(plain_term, bounded))
    slopes = -token_share * jnp.where(plain_term <= bounded, plain_term, 0.0)
    return (total_loss, slopes)


def combine(mine, theirs):
    top = jnp.maximum(mine[0], theirs[0])
    total = mine[1] * jnp.exp(mine[0] - top) + theirs[1] * jnp.exp(theirs[0] - top)
    return jnp.stack([top, total, mine[2] + theirs[2]])


def butterfly(stats):
    for axis in ("vocab", "grp"):
        size = lax.axis_size(axis)
        step = 1
        while step < size:
            perm = [(i, i ^ step) for i in range(size)]
            stats = combine(stats, lax.ppermute(stats, axis, perm))
            step *= 2
    return stats[0], stats[1], stats[2]


def doubling_gather(block, axis):
    size = lax.axis_size(axis)
    index = lax.axis_index(axis)
    step = 1
    while step < size:
        perm = [(i, i ^ step) for i in range(size)]
        theirs = lax.ppermute(block, axis, perm)
        upper = (index & step) != 0
        block = jnp.where(
            upper,
            jnp.concatenate([theirs, block], axis=0),
            jnp.concatenate([block, theirs], axis=0),
        )
        step *= 2
    return block


def shards(
    hidden, head_weight, targets, old_logprobs, loss_mask, beam_lengths, beam_group, rewards
):
    token_block = doubling_gather(hidden, "grp")
    features = lax.all_gather(token_block, "vocab", axis=1, tiled=True)
    shard = head_weight.shape[0]
    offset = (lax.axis_index("grp") * lax.axis_size("vocab") + lax.axis_index("vocab")) * shard
    vocab_ids = offset + jnp.arange(shard, dtype=jnp.int32)
    logits = lax.dot_general(
        features, head_weight, (((1,), (1,)), ((), ())), preferred_element_type=jnp.float32
    )
    hits = targets[:, None] == vocab_ids[None, :]
    picked = jnp.sum(jnp.where(hits, logits, 0.0), axis=1)
    local_top = jnp.max(logits, axis=1)
    local_sum = jnp.sum(jnp.exp(logits - local_top[:, None]), axis=1)
    top, total, target_logit = butterfly(jnp.stack([local_top, local_sum, picked]))
    log_total = top + jnp.log(total)
    logprob = target_logit - log_total
    total_loss, slopes = policy_terms(
        logprob, old_logprobs, loss_mask, beam_lengths, beam_group, rewards
    )
    grads = (
        slopes[:, None] * (hits.astype(jnp.float32) - jnp.exp(logits - log_total[:, None]))
    ).astype(jnp.bfloat16)
    head_grad = lax.dot_general(
        grads, features, (((0,), (0,)), ((), ())), preferred_element_type=jnp.float32
    )
    return (logprob, total_loss, head_grad.astype(jnp.bfloat16))


def solution(mesh):
    in_specs = (P("grp", "vocab"), P(("grp", "vocab"), None), P(), P(), P(), P(), P(), P())
    out_specs = (P(), P(), P(("grp", "vocab"), None))
    return jax.shard_map(shards, mesh=mesh, in_specs=in_specs, out_specs=out_specs, check_vma=False)
```

```python
import jax
import jax.numpy as jnp
from jax import lax
from jax.sharding import PartitionSpec as P

GROUP_BEAMS = 64


def policy_terms(logprob, old_logprobs, loss_mask, beam_lengths, beam_group, rewards):
    highest = lax.Precision.HIGHEST
    tok_count = logprob.shape[0]
    beam_count = beam_lengths.shape[0]
    group_count = beam_count // GROUP_BEAMS
    beam_ends = jnp.cumsum(beam_lengths)
    position = jnp.arange(tok_count, dtype=jnp.int32)
    beam_of = jnp.sum((position[:, None] >= beam_ends[None, :]).astype(jnp.int32), axis=1)
    token_beam = (beam_of[:, None] == jnp.arange(beam_count, dtype=jnp.int32)[None, :]).astype(
        jnp.float32
    )
    beam_onehot = (beam_group[:, None] == jnp.arange(group_count, dtype=jnp.int32)[None, :]).astype(
        jnp.float32
    )
    group_mean = jnp.dot(rewards, beam_onehot, precision=highest) / GROUP_BEAMS
    centred = rewards - jnp.dot(beam_onehot, group_mean, precision=highest)
    group_var = jnp.dot(centred * centred, beam_onehot, precision=highest) / GROUP_BEAMS
    advantage = centred / jnp.sqrt(jnp.dot(beam_onehot, group_var, precision=highest) + 1e-06)
    weight = loss_mask.astype(jnp.float32)
    counts = jnp.dot(weight, token_beam, precision=highest)
    token_adv = jnp.dot(token_beam, advantage, precision=highest)
    token_norm = jnp.dot(token_beam, jnp.maximum(counts, 1.0), precision=highest)
    ratios = jnp.exp(logprob - old_logprobs)
    clipped = jnp.clip(ratios, 0.8, 1.2)
    plain_term = ratios * token_adv
    bounded = clipped * token_adv
    token_share = weight / token_norm
    total_loss = -jnp.sum(token_share * jnp.minimum(plain_term, bounded))
    slopes = -token_share * jnp.where(plain_term <= bounded, plain_term, 0.0)
    return (total_loss, slopes)


def combine(mine, theirs):
    top = jnp.maximum(mine[0], theirs[0])
    total = mine[1] * jnp.exp(mine[0] - top) + theirs[1] * jnp.exp(theirs[0] - top)
    return jnp.stack([top, total, mine[2] + theirs[2]])


def butterfly(stats):
    for axis in ("vocab", "grp"):
        size = lax.axis_size(axis)
        step = 1
        while step < size:
            perm = [(i, i ^ step) for i in range(size)]
            stats = combine(stats, lax.ppermute(stats, axis, perm))
            step *= 2
    return stats[0], stats[1], stats[2]


def peer_gather(block, axis):
    size = lax.axis_size(axis)
    index = lax.axis_index(axis)
    got = [block] + [lax.ppermute(block, axis, [(i, i ^ k) for i in range(size)]) for k in range(1, size)]
    order = index ^ jnp.arange(size, dtype=jnp.int32)
    stacked = jnp.take(jnp.stack(got), order, axis=0)
    return stacked.reshape(size * block.shape[0], *block.shape[1:])


def shards(
    hidden, head_weight, targets, old_logprobs, loss_mask, beam_lengths, beam_group, rewards
):
    token_block = peer_gather(hidden, "grp")
    features = lax.all_gather(token_block, "vocab", axis=1, tiled=True)
    shard = head_weight.shape[0]
    offset = (lax.axis_index("grp") * lax.axis_size("vocab") + lax.axis_index("vocab")) * shard
    vocab_ids = offset + jnp.arange(shard, dtype=jnp.int32)
    logits = lax.dot_general(
        features, head_weight, (((1,), (1,)), ((), ())), preferred_element_type=jnp.float32
    )
    hits = targets[:, None] == vocab_ids[None, :]
    picked = jnp.sum(jnp.where(hits, logits, 0.0), axis=1)
    local_top = jnp.max(logits, axis=1)
    local_sum = jnp.sum(jnp.exp(logits - local_top[:, None]), axis=1)
    top, total, target_logit = butterfly(jnp.stack([local_top, local_sum, picked]))
    log_total = top + jnp.log(total)
    logprob = target_logit - log_total
    total_loss, slopes = policy_terms(
        logprob, old_logprobs, loss_mask, beam_lengths, beam_group, rewards
    )
    grads = (
        slopes[:, None] * (hits.astype(jnp.float32) - jnp.exp(logits - log_total[:, None]))
    ).astype(jnp.bfloat16)
    head_grad = lax.dot_general(
        grads, features, (((0,), (0,)), ((), ())), preferred_element_type=jnp.float32
    )
    return (logprob, total_loss, head_grad.astype(jnp.bfloat16))


def solution(mesh):
    in_specs = (P("grp", "vocab"), P(("grp", "vocab"), None), P(), P(), P(), P(), P(), P())
    out_specs = (P(), P(), P(("grp", "vocab"), None))
    return jax.shard_map(shards, mesh=mesh, in_specs=in_specs, out_specs=out_specs, check_vma=False)
```

```python
import jax
import jax.numpy as jnp
from jax import lax
from jax.sharding import PartitionSpec as P

GROUP_BEAMS = 64


def policy_terms(logprob, old_logprobs, loss_mask, beam_lengths, beam_group, rewards):
    highest = lax.Precision.HIGHEST
    tok_count = logprob.shape[0]
    beam_count = beam_lengths.shape[0]
    group_count = beam_count // GROUP_BEAMS
    beam_ends = jnp.cumsum(beam_lengths)
    position = jnp.arange(tok_count, dtype=jnp.int32)
    beam_of = jnp.sum((position[:, None] >= beam_ends[None, :]).astype(jnp.int32), axis=1)
    token_beam = (beam_of[:, None] == jnp.arange(beam_count, dtype=jnp.int32)[None, :]).astype(
        jnp.float32
    )
    beam_onehot = (beam_group[:, None] == jnp.arange(group_count, dtype=jnp.int32)[None, :]).astype(
        jnp.float32
    )
    group_mean = jnp.dot(rewards, beam_onehot, precision=highest) / GROUP_BEAMS
    centred = rewards - jnp.dot(beam_onehot, group_mean, precision=highest)
    group_var = jnp.dot(centred * centred, beam_onehot, precision=highest) / GROUP_BEAMS
    advantage = centred / jnp.sqrt(jnp.dot(beam_onehot, group_var, precision=highest) + 1e-06)
    weight = loss_mask.astype(jnp.float32)
    counts = jnp.dot(weight, token_beam, precision=highest)
    token_adv = jnp.dot(token_beam, advantage, precision=highest)
    token_norm = jnp.dot(token_beam, jnp.maximum(counts, 1.0), precision=highest)
    ratios = jnp.exp(logprob - old_logprobs)
    clipped = jnp.clip(ratios, 0.8, 1.2)
    plain_term = ratios * token_adv
    bounded = clipped * token_adv
    token_share = weight / token_norm
    total_loss = -jnp.sum(token_share * jnp.minimum(plain_term, bounded))
    slopes = -token_share * jnp.where(plain_term <= bounded, plain_term, 0.0)
    return (total_loss, slopes)


def combine(mine, theirs):
    top = jnp.maximum(mine[0], theirs[0])
    total = mine[1] * jnp.exp(mine[0] - top) + theirs[1] * jnp.exp(theirs[0] - top)
    return jnp.stack([top, total, mine[2] + theirs[2]])


def butterfly(stats):
    for axis in ("vocab", "grp"):
        size = lax.axis_size(axis)
        step = 1
        while step < size:
            perm = [(i, i ^ step) for i in range(size)]
            stats = combine(stats, lax.ppermute(stats, axis, perm))
            step *= 2
    return stats[0], stats[1], stats[2]


def peer_blocks(block, axis):
    size = lax.axis_size(axis)
    got = [block] + [lax.ppermute(block, axis, [(i, i ^ k) for i in range(size)]) for k in range(1, size)]
    return jnp.concatenate(got, axis=0)


def swap_blocks(values, axis, size):
    order = lax.axis_index("grp") ^ jnp.arange(size, dtype=jnp.int32)
    split = values.reshape(*values.shape[:axis], size, -1)
    return jnp.take(split, order, axis=axis).reshape(values.shape)


def shards(
    hidden, head_weight, targets, old_logprobs, loss_mask, beam_lengths, beam_group, rewards
):
    peers = lax.axis_size("grp")
    token_block = peer_blocks(hidden, "grp")
    features = lax.all_gather(token_block, "vocab", axis=1, tiled=True)
    shard = head_weight.shape[0]
    offset = (lax.axis_index("grp") * lax.axis_size("vocab") + lax.axis_index("vocab")) * shard
    vocab_ids = offset + jnp.arange(shard, dtype=jnp.int32)
    logits = lax.dot_general(
        features, head_weight, (((1,), (1,)), ((), ())), preferred_element_type=jnp.float32
    )
    hits = swap_blocks(targets, 0, peers)[:, None] == vocab_ids[None, :]
    picked = jnp.sum(jnp.where(hits, logits, 0.0), axis=1)
    local_top = jnp.max(logits, axis=1)
    local_sum = jnp.sum(jnp.exp(logits - local_top[:, None]), axis=1)
    stats = swap_blocks(jnp.stack([local_top, local_sum, picked]), 1, peers)
    top, total, target_logit = butterfly(stats)
    log_total = top + jnp.log(total)
    logprob = target_logit - log_total
    total_loss, slopes = policy_terms(
        logprob, old_logprobs, loss_mask, beam_lengths, beam_group, rewards
    )
    slopes = swap_blocks(slopes, 0, peers)
    log_total = swap_blocks(log_total, 0, peers)
    grads = (
        slopes[:, None] * (hits.astype(jnp.float32) - jnp.exp(logits - log_total[:, None]))
    ).astype(jnp.bfloat16)
    head_grad = lax.dot_general(
        grads, features, (((0,), (0,)), ((), ())), preferred_element_type=jnp.float32
    )
    return (logprob, total_loss, head_grad.astype(jnp.bfloat16))


def solution(mesh):
    in_specs = (P("grp", "vocab"), P(("grp", "vocab"), None), P(), P(), P(), P(), P(), P())
    out_specs = (P(), P(), P(("grp", "vocab"), None))
    return jax.shard_map(shards, mesh=mesh, in_specs=in_specs, out_specs=out_specs, check_vma=False)
```

```python
import jax
import jax.numpy as jnp
from jax import lax
from jax.sharding import PartitionSpec as P

GROUP_BEAMS = 64


def policy_terms(logprob, old_logprobs, loss_mask, beam_lengths, beam_group, rewards):
    highest = lax.Precision.HIGHEST
    tok_count = logprob.shape[0]
    beam_count = beam_lengths.shape[0]
    group_count = beam_count // GROUP_BEAMS
    beam_ends = jnp.cumsum(beam_lengths)
    position = jnp.arange(tok_count, dtype=jnp.int32)
    beam_of = jnp.sum((position[:, None] >= beam_ends[None, :]).astype(jnp.int32), axis=1)
    token_beam = (beam_of[:, None] == jnp.arange(beam_count, dtype=jnp.int32)[None, :]).astype(
        jnp.float32
    )
    beam_onehot = (beam_group[:, None] == jnp.arange(group_count, dtype=jnp.int32)[None, :]).astype(
        jnp.float32
    )
    group_mean = jnp.dot(rewards, beam_onehot, precision=highest) / GROUP_BEAMS
    centred = rewards - jnp.dot(beam_onehot, group_mean, precision=highest)
    group_var = jnp.dot(centred * centred, beam_onehot, precision=highest) / GROUP_BEAMS
    advantage = centred / jnp.sqrt(jnp.dot(beam_onehot, group_var, precision=highest) + 1e-06)
    weight = loss_mask.astype(jnp.float32)
    counts = jnp.dot(weight, token_beam, precision=highest)
    token_adv = jnp.dot(token_beam, advantage, precision=highest)
    token_norm = jnp.dot(token_beam, jnp.maximum(counts, 1.0), precision=highest)
    ratios = jnp.exp(logprob - old_logprobs)
    clipped = jnp.clip(ratios, 0.8, 1.2)
    plain_term = ratios * token_adv
    bounded = clipped * token_adv
    token_share = weight / token_norm
    total_loss = -jnp.sum(token_share * jnp.minimum(plain_term, bounded))
    slopes = -token_share * jnp.where(plain_term <= bounded, plain_term, 0.0)
    return (total_loss, slopes)


def combine(mine, theirs):
    top = jnp.maximum(mine[0], theirs[0])
    total = mine[1] * jnp.exp(mine[0] - top) + theirs[1] * jnp.exp(theirs[0] - top)
    return jnp.stack([top, total, mine[2] + theirs[2]])


def butterfly(stats):
    for axis, masks in (("vocab", (1, 2, 4, 12)), ("grp", (1, 3, 4))):
        size = lax.axis_size(axis)
        for mask in masks:
            perm = [(i, i ^ mask) for i in range(size)]
            stats = combine(stats, lax.ppermute(stats, axis, perm))
    return stats[0], stats[1], stats[2]


def peer_gather(block, axis):
    size = lax.axis_size(axis)
    index = lax.axis_index(axis)
    got = [block] + [lax.ppermute(block, axis, [(i, i ^ k) for i in range(size)]) for k in range(1, size)]
    order = index ^ jnp.arange(size, dtype=jnp.int32)
    stacked = jnp.take(jnp.stack(got), order, axis=0)
    return stacked.reshape(size * block.shape[0], *block.shape[1:])


def shards(
    hidden, head_weight, targets, old_logprobs, loss_mask, beam_lengths, beam_group, rewards
):
    token_block = peer_gather(hidden, "grp")
    features = lax.all_gather(token_block, "vocab", axis=1, tiled=True)
    shard = head_weight.shape[0]
    offset = (lax.axis_index("grp") * lax.axis_size("vocab") + lax.axis_index("vocab")) * shard
    vocab_ids = offset + jnp.arange(shard, dtype=jnp.int32)
    logits = lax.dot_general(
        features, head_weight, (((1,), (1,)), ((), ())), preferred_element_type=jnp.float32
    )
    hits = targets[:, None] == vocab_ids[None, :]
    picked = jnp.sum(jnp.where(hits, logits, 0.0), axis=1)
    local_top = jnp.max(logits, axis=1)
    local_sum = jnp.sum(jnp.exp(logits - local_top[:, None]), axis=1)
    top, total, target_logit = butterfly(jnp.stack([local_top, local_sum, picked]))
    log_total = top + jnp.log(total)
    logprob = target_logit - log_total
    total_loss, slopes = policy_terms(
        logprob, old_logprobs, loss_mask, beam_lengths, beam_group, rewards
    )
    grads = (
        slopes[:, None] * (hits.astype(jnp.float32) - jnp.exp(logits - log_total[:, None]))
    ).astype(jnp.bfloat16)
    head_grad = lax.dot_general(
        grads, features, (((0,), (0,)), ((), ())), preferred_element_type=jnp.float32
    )
    return (logprob, total_loss, head_grad.astype(jnp.bfloat16))


def solution(mesh):
    in_specs = (P("grp", "vocab"), P(("grp", "vocab"), None), P(), P(), P(), P(), P(), P())
    out_specs = (P(), P(), P(("grp", "vocab"), None))
    return jax.shard_map(shards, mesh=mesh, in_specs=in_specs, out_specs=out_specs, check_vma=False)
```

```python
import jax
import jax.numpy as jnp
from jax import lax
from jax.sharding import PartitionSpec as P

GROUP_BEAMS = 64


def policy_terms(logprob, old_logprobs, loss_mask, beam_lengths, beam_group, rewards):
    highest = lax.Precision.HIGHEST
    tok_count = logprob.shape[0]
    beam_count = beam_lengths.shape[0]
    group_count = beam_count // GROUP_BEAMS
    beam_ends = jnp.cumsum(beam_lengths)
    position = jnp.arange(tok_count, dtype=jnp.int32)
    beam_of = jnp.sum((position[:, None] >= beam_ends[None, :]).astype(jnp.int32), axis=1)
    token_beam = (beam_of[:, None] == jnp.arange(beam_count, dtype=jnp.int32)[None, :]).astype(
        jnp.float32
    )
    beam_onehot = (beam_group[:, None] == jnp.arange(group_count, dtype=jnp.int32)[None, :]).astype(
        jnp.float32
    )
    group_mean = jnp.dot(rewards, beam_onehot, precision=highest) / GROUP_BEAMS
    centred = rewards - jnp.dot(beam_onehot, group_mean, precision=highest)
    group_var = jnp.dot(centred * centred, beam_onehot, precision=highest) / GROUP_BEAMS
    advantage = centred / jnp.sqrt(jnp.dot(beam_onehot, group_var, precision=highest) + 1e-06)
    weight = loss_mask.astype(jnp.float32)
    counts = jnp.dot(weight, token_beam, precision=highest)
    token_adv = jnp.dot(token_beam, advantage, precision=highest)
    token_norm = jnp.dot(token_beam, jnp.maximum(counts, 1.0), precision=highest)
    ratios = jnp.exp(logprob - old_logprobs)
    clipped = jnp.clip(ratios, 0.8, 1.2)
    plain_term = ratios * token_adv
    bounded = clipped * token_adv
    token_share = weight / token_norm
    total_loss = -jnp.sum(token_share * jnp.minimum(plain_term, bounded))
    slopes = -token_share * jnp.where(plain_term <= bounded, plain_term, 0.0)
    return (total_loss, slopes)


def combine(mine, theirs):
    top = jnp.maximum(mine[0], theirs[0])
    total = mine[1] * jnp.exp(mine[0] - top) + theirs[1] * jnp.exp(theirs[0] - top)
    return jnp.stack([top, total, mine[2] + theirs[2]])


def butterfly(stats):
    for axis, masks in (("vocab", (1, 2, 4, 12)), ("grp", (1, 3, 4))):
        size = lax.axis_size(axis)
        for mask in masks:
            perm = [(i, i ^ mask) for i in range(size)]
            stats = combine(stats, lax.ppermute(stats, axis, perm))
    return stats[0], stats[1], stats[2]


def peer_gather(block, axis):
    size = lax.axis_size(axis)
    repeated = jnp.broadcast_to(block[None], (size,) + block.shape)
    gathered = lax.all_to_all(repeated, axis, 0, 0, tiled=False)
    return gathered.reshape(size * block.shape[0], *block.shape[1:])


def shards(
    hidden, head_weight, targets, old_logprobs, loss_mask, beam_lengths, beam_group, rewards
):
    token_block = peer_gather(hidden, "grp")
    features = lax.all_gather(token_block, "vocab", axis=1, tiled=True)
    shard = head_weight.shape[0]
    offset = (lax.axis_index("grp") * lax.axis_size("vocab") + lax.axis_index("vocab")) * shard
    vocab_ids = offset + jnp.arange(shard, dtype=jnp.int32)
    logits = lax.dot_general(
        features, head_weight, (((1,), (1,)), ((), ())), preferred_element_type=jnp.float32
    )
    hits = targets[:, None] == vocab_ids[None, :]
    picked = jnp.sum(jnp.where(hits, logits, 0.0), axis=1)
    local_top = jnp.max(logits, axis=1)
    local_sum = jnp.sum(jnp.exp(logits - local_top[:, None]), axis=1)
    top, total, target_logit = butterfly(jnp.stack([local_top, local_sum, picked]))
    log_total = top + jnp.log(total)
    logprob = target_logit - log_total
    total_loss, slopes = policy_terms(
        logprob, old_logprobs, loss_mask, beam_lengths, beam_group, rewards
    )
    grads = (
        slopes[:, None] * (hits.astype(jnp.float32) - jnp.exp(logits - log_total[:, None]))
    ).astype(jnp.bfloat16)
    head_grad = lax.dot_general(
        grads, features, (((0,), (0,)), ((), ())), preferred_element_type=jnp.float32
    )
    return (logprob, total_loss, head_grad.astype(jnp.bfloat16))


def solution(mesh):
    in_specs = (P("grp", "vocab"), P(("grp", "vocab"), None), P(), P(), P(), P(), P(), P())
    out_specs = (P(), P(), P(("grp", "vocab"), None))
    return jax.shard_map(shards, mesh=mesh, in_specs=in_specs, out_specs=out_specs, check_vma=False)
```

```python
import jax
import jax.numpy as jnp
from jax import lax
from jax.sharding import PartitionSpec as P

GROUP_BEAMS = 64


def policy_terms(logprob, old_logprobs, loss_mask, beam_lengths, beam_group, rewards):
    highest = lax.Precision.HIGHEST
    tok_count = logprob.shape[0]
    beam_count = beam_lengths.shape[0]
    group_count = beam_count // GROUP_BEAMS
    beam_ends = jnp.cumsum(beam_lengths)
    position = jnp.arange(tok_count, dtype=jnp.int32)
    beam_of = jnp.sum((position[:, None] >= beam_ends[None, :]).astype(jnp.int32), axis=1)
    token_beam = (beam_of[:, None] == jnp.arange(beam_count, dtype=jnp.int32)[None, :]).astype(
        jnp.float32
    )
    beam_onehot = (beam_group[:, None] == jnp.arange(group_count, dtype=jnp.int32)[None, :]).astype(
        jnp.float32
    )
    group_mean = jnp.dot(rewards, beam_onehot, precision=highest) / GROUP_BEAMS
    centred = rewards - jnp.dot(beam_onehot, group_mean, precision=highest)
    group_var = jnp.dot(centred * centred, beam_onehot, precision=highest) / GROUP_BEAMS
    advantage = centred / jnp.sqrt(jnp.dot(beam_onehot, group_var, precision=highest) + 1e-06)
    weight = loss_mask.astype(jnp.float32)
    counts = jnp.dot(weight, token_beam, precision=highest)
    token_adv = jnp.dot(token_beam, advantage, precision=highest)
    token_norm = jnp.dot(token_beam, jnp.maximum(counts, 1.0), precision=highest)
    ratios = jnp.exp(logprob - old_logprobs)
    clipped = jnp.clip(ratios, 0.8, 1.2)
    plain_term = ratios * token_adv
    bounded = clipped * token_adv
    token_share = weight / token_norm
    total_loss = -jnp.sum(token_share * jnp.minimum(plain_term, bounded))
    slopes = -token_share * jnp.where(plain_term <= bounded, plain_term, 0.0)
    return (total_loss, slopes)


def combine(mine, theirs):
    top = jnp.maximum(mine[0], theirs[0])
    total = mine[1] * jnp.exp(mine[0] - top) + theirs[1] * jnp.exp(theirs[0] - top)
    return jnp.stack([top, total, mine[2] + theirs[2]])


def combine_all(gathered):
    top = jnp.max(gathered[:, 0], axis=0)
    total = jnp.sum(gathered[:, 1] * jnp.exp(gathered[:, 0] - top), axis=0)
    return jnp.stack([top, total, jnp.sum(gathered[:, 2], axis=0)])


def butterfly(stats):
    size = lax.axis_size("vocab")
    repeated = jnp.broadcast_to(stats[None], (size,) + stats.shape)
    stats = combine_all(lax.all_to_all(repeated, "vocab", 0, 0, tiled=False))
    size = lax.axis_size("grp")
    for mask in (1, 3, 4):
        perm = [(i, i ^ mask) for i in range(size)]
        stats = combine(stats, lax.ppermute(stats, "grp", perm))
    return stats[0], stats[1], stats[2]


def peer_gather(block, axis):
    size = lax.axis_size(axis)
    index = lax.axis_index(axis)
    got = [block] + [lax.ppermute(block, axis, [(i, i ^ k) for i in range(size)]) for k in range(1, size)]
    order = index ^ jnp.arange(size, dtype=jnp.int32)
    stacked = jnp.take(jnp.stack(got), order, axis=0)
    return stacked.reshape(size * block.shape[0], *block.shape[1:])


def shards(
    hidden, head_weight, targets, old_logprobs, loss_mask, beam_lengths, beam_group, rewards
):
    token_block = peer_gather(hidden, "grp")
    features = lax.all_gather(token_block, "vocab", axis=1, tiled=True)
    shard = head_weight.shape[0]
    offset = (lax.axis_index("grp") * lax.axis_size("vocab") + lax.axis_index("vocab")) * shard
    vocab_ids = offset + jnp.arange(shard, dtype=jnp.int32)
    logits = lax.dot_general(
        features, head_weight, (((1,), (1,)), ((), ())), preferred_element_type=jnp.float32
    )
    hits = targets[:, None] == vocab_ids[None, :]
    picked = jnp.sum(jnp.where(hits, logits, 0.0), axis=1)
    local_top = jnp.max(logits, axis=1)
    local_sum = jnp.sum(jnp.exp(logits - local_top[:, None]), axis=1)
    top, total, target_logit = butterfly(jnp.stack([local_top, local_sum, picked]))
    log_total = top + jnp.log(total)
    logprob = target_logit - log_total
    total_loss, slopes = policy_terms(
        logprob, old_logprobs, loss_mask, beam_lengths, beam_group, rewards
    )
    grads = (
        slopes[:, None] * (hits.astype(jnp.float32) - jnp.exp(logits - log_total[:, None]))
    ).astype(jnp.bfloat16)
    head_grad = lax.dot_general(
        grads, features, (((0,), (0,)), ((), ())), preferred_element_type=jnp.float32
    )
    return (logprob, total_loss, head_grad.astype(jnp.bfloat16))


def solution(mesh):
    in_specs = (P("grp", "vocab"), P(("grp", "vocab"), None), P(), P(), P(), P(), P(), P())
    out_specs = (P(), P(), P(("grp", "vocab"), None))
    return jax.shard_map(shards, mesh=mesh, in_specs=in_specs, out_specs=out_specs, check_vma=False)
```
